256 devices in a mesh: island: 4 (over x_lo, core), fsdp: 64 (over x_hi, z, y).
Axes of the slice: x: 4 (x_hi: 2, x_lo: 2; x = x_hi * 2 + x_lo), y: 4, z: 8, core: 2. Of those that a mesh axis runs over, the one named last changes fastest.
Arguments:
- acts: bfloat16 [65536, 8192], P(('island', 'fsdp')), may hold values from -24 to 24
- cotangent: bfloat16 [65536, 512], P(('island', 'fsdp')), may hold values from -6 to 6
- global_params: float32 [8192, 512], P('fsdp'), may hold values from -0.12 to 0.12
- momentum: float32 [8192, 512], P('fsdp'), may hold values from -0.18 to 0.18
- island_drift: float32 [4, 8192, 512], P('island', 'fsdp'), may hold values from -0.12 to 0.12
- moment1: float32 [4, 8192, 512], P('island', 'fsdp'), may hold values from -6 to 6
- moment2: float32 [4, 8192, 512], P('island', 'fsdp'), may hold values from 0.05 to 1
Outputs:
- keys: bfloat16 [65536, 512], P(('island', 'fsdp'))
- new_global: float32 [8192, 512], P('fsdp')
- new_momentum: float32 [8192, 512], P('fsdp')
- moment1_out: float32 [4, 8192, 512], P('island', 'fsdp')
- moment2_out: float32 [4, 8192, 512], P('island', 'fsdp')
The draws below stay inside these ranges and needn't reach their ends.
All inputs are finite; a program needn't handle non-finite values.
Results may differ from the reference program's by a relative error of at most 0.0049.
Values may be sent and summed in bfloat16 or wider, within the bound.
No kernel may reach another device: no remote copies, remote signals or barrier semaphores. Data moves between devices by JAX's collectives and lax.ppermute only.
A program may use at most 128 MiB of HBM per device.

```python
import math
import jax
import jax.numpy as jnp

D = 8192
TOK_DEV = 256
KW = 512
TOKENS = 65536
N_ISLAND = 4
N_FSDP = 64


def strengthened(values, rng, source, target, blocks, factor):
    owner, partner = [(jnp.arange(values.shape[dim]) // (values.shape[dim] // blocks)).reshape([-1 if axis == dim else 1 for axis in range(values.ndim)]) for dim in (source, target)]
    chosen = jax.random.permutation(rng, blocks)[partner]
    strong = (owner == chosen) | (owner == (partner + blocks // 2) % blocks)
    return jnp.where(strong, factor * values, values)


def level_of(own_key, extent, split, low, top_value):
    factor_of = 1.0
    for dim, parts in split:
        draws = jax.random.uniform(jax.random.fold_in(jax.random.fold_in(own_key, 6), dim), (parts,), jnp.float32, low / len(split), top_value / len(split))
        factor_of = factor_of * jnp.repeat(jnp.exp(draws), extent[dim] // parts).reshape((-1,) + (1,) * (len(extent) - 1 - dim))
    return factor_of


def centred(key, extent, scale, most, shards=(), held_as=jnp.bfloat16):
    loudness = level_of(key, extent, shards, -0.22, 0.18) if shards else 1.0
    values = jax.random.normal(key, extent, jnp.float32) * scale * loudness
    return jnp.minimum(jnp.maximum(values, -most), most).astype(held_as)


def gaussian_with(own_key, dims, spread, most, pieces, heavy, held_as=jnp.bfloat16):
    result = spread * jax.random.normal(own_key, dims, jnp.float32)
    if pieces:
        result = result * level_of(own_key, dims, pieces, -0.22, 0.18)
    return jnp.clip(strengthened(result, jax.random.fold_in(own_key, 3), *heavy), -most, most).astype(held_as)


def setup_inputs(seed: int = 0) -> dict:
    seeds = jax.random.split(jax.random.key(seed), 8)
    acts = gaussian_with(seeds[0], (TOKENS, D), 1.0, 24.0, ((0, 256),), (0, 1, 256, 6.0))
    cotangent = centred(seeds[1], (TOKENS, KW), 1.0, 6.0, ((0, 256),))
    global_params = centred(seeds[2], (D, KW), 0.02, 0.12, ((0, 64),), jnp.float32)
    momentum = centred(seeds[3], (D, KW), 0.03, 0.18, ((0, 64),), jnp.float32)
    island_drift = centred(seeds[4], (N_ISLAND, D, KW), 0.02, 0.12, ((0, 4), (1, 64)), jnp.float32)
    moment1 = centred(seeds[5], (N_ISLAND, D, KW), 1.0, 6.0, ((0, 4), (1, 64)), jnp.float32)
    moment2 = jnp.clip(jnp.exp(math.log(1.0) - 2.9957323 * jax.random.uniform(seeds[6], (N_ISLAND, D, KW), jnp.float32) ** level_of(seeds[6], (N_ISLAND, D, KW), ((0, 4), (1, 64)), -0.2, 0.2)), 0.05, 1.0)
    return dict(acts=acts, cotangent=cotangent, global_params=global_params, momentum=momentum, island_drift=island_drift, moment1=moment1, moment2=moment2)


beta_one = 0.9
beta_two = 0.95
epsilon = 1e-08
inner_rate = 0.05
decay_rate = 0.1
outer_rate = 0.7
nesterov = 0.9

def reference(acts, cotangent, global_params, momentum, island_drift, moment1, moment2):
    count = TOK_DEV * N_FSDP
    scale = count ** (-0.5)
    first_list = []
    second_list = []
    total = jnp.zeros((D, KW), jnp.float32)
    for island in range(N_ISLAND):
        rows_x = acts[island * count:(island + 1) * count]
        rows_c = cotangent[island * count:(island + 1) * count]
        grad = jnp.dot(rows_x.T, rows_c, preferred_element_type=jnp.float32) * scale
        first = beta_one * moment1[island] + (1.0 - beta_one) * grad
        second = beta_two * moment2[island] + (1.0 - beta_two) * grad * grad
        step = first / (jnp.sqrt(second) + epsilon) + decay_rate * (global_params - island_drift[island])
        pseudo = island_drift[island] + inner_rate * step
        total = total + pseudo
        first_list.append(first)
        second_list.append(second)
    mean = total / N_ISLAND
    new_momentum = nesterov * momentum + mean
    new_global = global_params - outer_rate * (mean + nesterov * new_momentum)
    weights = new_global.astype(jnp.bfloat16)
    keys = (jnp.dot(acts, weights, preferred_element_type=jnp.float32) * D ** (-0.5)).astype(jnp.bfloat16)
    return (keys, new_global, new_momentum, jnp.stack(first_list), jnp.stack(second_list))
```

```python
import jax
import jax.numpy as jnp
from jax import lax
from jax.sharding import Mesh, PartitionSpec as P

D = 8192
FS = ("xh", "z", "y")


beta_one = 0.9
beta_two = 0.95
epsilon = 1e-08
inner_rate = 0.05
decay_rate = 0.1
outer_rate = 0.7
nesterov = 0.9


def per_device(acts, cotangent, global_params, momentum, island_drift, moment1, moment2):
    fsdp_count = lax.axis_size(FS)
    island_count = lax.axis_size("island")
    scale = (acts.shape[0] * fsdp_count) ** (-0.5)
    xh_n, z_n, y_n = (lax.axis_size(a) for a in ("xh", "z", "y"))
    tokens = acts.shape[0]
    acts_perm = (
        acts.reshape(tokens, xh_n, z_n, D // (xh_n * z_n))
        .transpose(0, 2, 1, 3)
        .reshape(tokens, D)
    )
    partial = lax.dot_general(
        acts_perm, cotangent, (((0,), (0,)), ((), ())), preferred_element_type=jnp.float32
    )
    grad = lax.psum_scatter(partial, "z", scatter_dimension=0, tiled=True)
    grad = lax.psum_scatter(grad, "xh", scatter_dimension=0, tiled=True)
    grad = lax.psum_scatter(grad, "y", scatter_dimension=0, tiled=True)
    grad = grad * scale
    drift = island_drift[0]
    first = beta_one * moment1[0] + (1.0 - beta_one) * grad
    second = beta_two * moment2[0] + (1.0 - beta_two) * grad * grad
    step = first / (jnp.sqrt(second) + epsilon) + decay_rate * (global_params - drift)
    pseudo = drift + inner_rate * step
    pair_core = [(i, i ^ 1) for i in range(island_count)]
    pair_chip = [(i, i ^ 2) for i in range(island_count)]
    summed = pseudo + lax.ppermute(pseudo, "island", pair_core)
    summed = summed + lax.ppermute(summed, "island", pair_chip)
    mean = summed / island_count
    new_momentum = nesterov * momentum + mean
    new_global = global_params - outer_rate * (mean + nesterov * new_momentum)
    weights = new_global.astype(jnp.bfloat16)
    core = lax.axis_index("island") % 2
    half = weights.shape[1] // 2
    own = lax.dynamic_slice_in_dim(weights, core * half, half, axis=1)
    own_full = lax.all_gather(own, FS, axis=0, tiled=True)
    other_full = lax.ppermute(own_full, "island", pair_core)
    keys_own = jnp.dot(acts, own_full, preferred_element_type=jnp.float32)
    keys_other = jnp.dot(acts, other_full, preferred_element_type=jnp.float32)
    keys_own = (keys_own * D ** (-0.5)).astype(jnp.bfloat16)
    keys_other = (keys_other * D ** (-0.5)).astype(jnp.bfloat16)
    is_first = core == 0
    keys = jnp.concatenate(
        [jnp.where(is_first, keys_own, keys_other), jnp.where(is_first, keys_other, keys_own)],
        axis=1,
    )
    return (keys, new_global, new_momentum, first[None], second[None])


def solution(mesh):
    fsdp_n = mesh.shape["fsdp"]
    mesh = Mesh(mesh.devices.reshape(mesh.shape["island"], 2, 8, fsdp_n // 16), ("island",) + FS)
    return jax.shard_map(
        per_device,
        mesh=mesh,
        in_specs=(
            P(("island", *FS), None),
            P(("island", *FS), None),
            P(FS, None),
            P(FS, None),
            P("island", FS, None),
            P("island", FS, None),
            P("island", FS, None),
        ),
        out_specs=(
            P(("island", *FS), None),
            P(FS, None),
            P(FS, None),
            P("island", FS, None),
            P("island", FS, None),
        ),
        check_vma=False,
    )
```

```python
import jax
import jax.numpy as jnp
from jax import lax
from jax.sharding import Mesh, PartitionSpec as P

D = 8192
FS = ("xh", "z", "y")


beta_one = 0.9
beta_two = 0.95
epsilon = 1e-08
inner_rate = 0.05
decay_rate = 0.1
outer_rate = 0.7
nesterov = 0.9


def per_device(acts, cotangent, global_params, momentum, island_drift, moment1, moment2):
    fsdp_count = lax.axis_size(FS)
    island_count = lax.axis_size("island")
    scale = (acts.shape[0] * fsdp_count) ** (-0.5)
    xh_n, z_n, y_n = (lax.axis_size(a) for a in ("xh", "z", "y"))
    tokens = acts.shape[0]
    acts_perm = (
        acts.reshape(tokens, xh_n, z_n, D // (xh_n * z_n))
        .transpose(0, 2, 1, 3)
        .reshape(tokens, D)
    )
    partial = lax.dot_general(
        acts_perm, cotangent, (((0,), (0,)), ((), ())), preferred_element_type=jnp.float32
    )
    grad = lax.psum_scatter(partial, "z", scatter_dimension=0, tiled=True)
    grad = lax.psum_scatter(grad, "xh", scatter_dimension=0, tiled=True)
    grad = lax.psum_scatter(grad, "y", scatter_dimension=0, tiled=True)
    grad = grad * scale
    drift = island_drift[0]
    first = beta_one * moment1[0] + (1.0 - beta_one) * grad
    second = beta_two * moment2[0] + (1.0 - beta_two) * grad * grad
    step = first / (jnp.sqrt(second) + epsilon) + decay_rate * (global_params - drift)
    pseudo = drift + inner_rate * step
    pair_core = [(i, i ^ 1) for i in range(island_count)]
    pair_chip = [(i, i ^ 2) for i in range(island_count)]
    summed = pseudo + lax.ppermute(pseudo, "island", pair_core)
    summed = summed + lax.ppermute(summed, "island", pair_chip)
    mean = summed / island_count
    new_momentum = nesterov * momentum + mean
    new_global = global_params - outer_rate * (mean + nesterov * new_momentum)
    weights = new_global.astype(jnp.bfloat16)
    core = lax.axis_index("island") % 2
    half = weights.shape[1] // 2
    own = lax.dynamic_slice_in_dim(weights, core * half, half, axis=1)
    own_full = lax.all_gather(own, "y", axis=0, tiled=True)
    own_full = lax.all_gather(own_full, "xh", axis=0, tiled=True)
    own_full = lax.all_gather(own_full, "z", axis=0, tiled=True)
    other_full = lax.ppermute(own_full, "island", pair_core)
    keys_own = jnp.dot(acts_perm, own_full, preferred_element_type=jnp.float32)
    keys_other = jnp.dot(acts_perm, other_full, preferred_element_type=jnp.float32)
    keys_own = (keys_own * D ** (-0.5)).astype(jnp.bfloat16)
    keys_other = (keys_other * D ** (-0.5)).astype(jnp.bfloat16)
    is_first = core == 0
    keys = jnp.concatenate(
        [jnp.where(is_first, keys_own, keys_other), jnp.where(is_first, keys_other, keys_own)],
        axis=1,
    )
    return (keys, new_global, new_momentum, first[None], second[None])


def solution(mesh):
    fsdp_n = mesh.shape["fsdp"]
    mesh = Mesh(mesh.devices.reshape(mesh.shape["island"], 2, 8, fsdp_n // 16), ("island",) + FS)
    return jax.shard_map(
        per_device,
        mesh=mesh,
        in_specs=(
            P(("island", *FS), None),
            P(("island", *FS), None),
            P(FS, None),
            P(FS, None),
            P("island", FS, None),
            P("island", FS, None),
            P("island", FS, None),
        ),
        out_specs=(
            P(("island", *FS), None),
            P(FS, None),
            P(FS, None),
            P("island", FS, None),
            P("island", FS, None),
        ),
        check_vma=False,
    )
```

```python
import jax
import jax.numpy as jnp
from jax import lax
from jax.sharding import Mesh, PartitionSpec as P

D = 8192
FS = ("xh", "z", "y")


beta_one = 0.9
beta_two = 0.95
epsilon = 1e-08
inner_rate = 0.05
decay_rate = 0.1
outer_rate = 0.7
nesterov = 0.9


def halving_scatter(x, axis):
    n = lax.axis_size(axis)
    me = lax.axis_index(axis)
    bit = n // 2
    while bit >= 1:
        half = x.shape[0] // 2
        mine = (me // bit) % 2
        keep = lax.dynamic_slice_in_dim(x, mine * half, half, axis=0)
        send = lax.dynamic_slice_in_dim(x, (1 - mine) * half, half, axis=0)
        recv = lax.ppermute(send, axis, [(i, i ^ bit) for i in range(n)])
        x = keep + recv
        bit //= 2
    return x


def doubling_gather(x, axis):
    n = lax.axis_size(axis)
    me = lax.axis_index(axis)
    bit = 1
    while bit < n:
        recv = lax.ppermute(x, axis, [(i, i ^ bit) for i in range(n)])
        low = (me // bit) % 2 == 0
        x = jnp.where(low, jnp.concatenate([x, recv], 0), jnp.concatenate([recv, x], 0))
        bit *= 2
    return x


def per_device(acts, cotangent, global_params, momentum, island_drift, moment1, moment2):
    fsdp_count = lax.axis_size(FS)
    island_count = lax.axis_size("island")
    scale = (acts.shape[0] * fsdp_count) ** (-0.5)
    xh_n, z_n, y_n = (lax.axis_size(a) for a in ("xh", "z", "y"))
    tokens = acts.shape[0]
    acts_perm = (
        acts.reshape(tokens, xh_n, z_n, D // (xh_n * z_n))
        .transpose(0, 2, 1, 3)
        .reshape(tokens, D)
    )
    partial = lax.dot_general(
        acts_perm, cotangent, (((0,), (0,)), ((), ())), preferred_element_type=jnp.float32
    )
    grad = lax.psum_scatter(partial, "z", scatter_dimension=0, tiled=True)
    grad = halving_scatter(grad, "xh")
    grad = halving_scatter(grad, "y")
    grad = grad * scale
    drift = island_drift[0]
    first = beta_one * moment1[0] + (1.0 - beta_one) * grad
    second = beta_two * moment2[0] + (1.0 - beta_two) * grad * grad
    step = first / (jnp.sqrt(second) + epsilon) + decay_rate * (global_params - drift)
    pseudo = drift + inner_rate * step
    pair_core = [(i, i ^ 1) for i in range(island_count)]
    pair_chip = [(i, i ^ 2) for i in range(island_count)]
    summed = pseudo + lax.ppermute(pseudo, "island", pair_core)
    summed = summed + lax.ppermute(summed, "island", pair_chip)
    mean = summed / island_count
    new_momentum = nesterov * momentum + mean
    new_global = global_params - outer_rate * (mean + nesterov * new_momentum)
    weights = new_global.astype(jnp.bfloat16)
    core = lax.axis_index("island") % 2
    half = weights.shape[1] // 2
    own = lax.dynamic_slice_in_dim(weights, core * half, half, axis=1)
    own_full = doubling_gather(own, "y")
    own_full = doubling_gather(own_full, "xh")
    own_full = lax.all_gather(own_full, "z", axis=0, tiled=True)
    other_full = lax.ppermute(own_full, "island", pair_core)
    keys_own = jnp.dot(acts_perm, own_full, preferred_element_type=jnp.float32)
    keys_other = jnp.dot(acts_perm, other_full, preferred_element_type=jnp.float32)
    keys_own = (keys_own * D ** (-0.5)).astype(jnp.bfloat16)
    keys_other = (keys_other * D ** (-0.5)).astype(jnp.bfloat16)
    is_first = core == 0
    keys = jnp.concatenate(
        [jnp.where(is_first, keys_own, keys_other), jnp.where(is_first, keys_other, keys_own)],
        axis=1,
    )
    return (keys, new_global, new_momentum, first[None], second[None])


def solution(mesh):
    fsdp_n = mesh.shape["fsdp"]
    mesh = Mesh(mesh.devices.reshape(mesh.shape["island"], 2, 8, fsdp_n // 16), ("island",) + FS)
    return jax.shard_map(
        per_device,
        mesh=mesh,
        in_specs=(
            P(("island", *FS), None),
            P(("island", *FS), None),
            P(FS, None),
            P(FS, None),
            P("island", FS, None),
            P("island", FS, None),
            P("island", FS, None),
        ),
        out_specs=(
            P(("island", *FS), None),
            P(FS, None),
            P(FS, None),
            P("island", FS, None),
            P("island", FS, None),
        ),
        check_vma=False,
    )
```

```python
import jax
import jax.numpy as jnp
from jax import lax
from jax.sharding import Mesh, PartitionSpec as P

D = 8192
FS = ("xh", "z", "y")


beta_one = 0.9
beta_two = 0.95
epsilon = 1e-08
inner_rate = 0.05
decay_rate = 0.1
outer_rate = 0.7
nesterov = 0.9


def ring_scatter(x, axis):
    n = lax.axis_size(axis)
    me = lax.axis_index(axis)
    chunk = x.shape[0] // n
    h = x.shape[1] // 2
    parts = []
    for sign, cols in ((1, slice(0, h)), (-1, slice(h, None))):
        data = x[:, cols]
        perm = [(i, (i + sign) % n) for i in range(n)]
        pick = lambda k: lax.dynamic_slice_in_dim(data, (k % n) * chunk, chunk, axis=0)
        acc = pick(me - sign + n)
        for s in range(n - 1):
            acc = lax.ppermute(acc, axis, perm) + pick(me - sign * (2 + s) + 2 * n)
        parts.append(acc)
    return jnp.concatenate(parts, axis=1)


def halving_scatter(x, axis):
    n = lax.axis_size(axis)
    me = lax.axis_index(axis)
    bit = n // 2
    while bit >= 1:
        half = x.shape[0] // 2
        mine = (me // bit) % 2
        keep = lax.dynamic_slice_in_dim(x, mine * half, half, axis=0)
        send = lax.dynamic_slice_in_dim(x, (1 - mine) * half, half, axis=0)
        recv = lax.ppermute(send, axis, [(i, i ^ bit) for i in range(n)])
        x = keep + recv
        bit //= 2
    return x


def doubling_gather(x, axis):
    n = lax.axis_size(axis)
    me = lax.axis_index(axis)
    bit = 1
    while bit < n:
        recv = lax.ppermute(x, axis, [(i, i ^ bit) for i in range(n)])
        low = (me // bit) % 2 == 0
        x = jnp.where(low, jnp.concatenate([x, recv], 0), jnp.concatenate([recv, x], 0))
        bit *= 2
    return x


def per_device(acts, cotangent, global_params, momentum, island_drift, moment1, moment2):
    fsdp_count = lax.axis_size(FS)
    island_count = lax.axis_size("island")
    scale = (acts.shape[0] * fsdp_count) ** (-0.5)
    xh_n, z_n, y_n = (lax.axis_size(a) for a in ("xh", "z", "y"))
    tokens = acts.shape[0]
    blocks = acts.reshape(tokens, xh_n, z_n, y_n, D // (xh_n * z_n * y_n))
    acts_perm = blocks.transpose(0, 2, 1, 3, 4).reshape(tokens, D)
    acts_yfirst = blocks.transpose(0, 3, 2, 1, 4).reshape(tokens, D)
    cols = cotangent.shape[1] // 2
    dims = (((0,), (0,)), ((), ()))
    part_z = lax.dot_general(acts_perm, cotangent[:, :cols], dims, preferred_element_type=jnp.float32)
    part_y = lax.dot_general(acts_yfirst, cotangent[:, cols:], dims, preferred_element_type=jnp.float32)
    grad_z = lax.psum_scatter(part_z, "z", scatter_dimension=0, tiled=True)
    grad_y = ring_scatter(part_y, "y")
    grad_z = halving_scatter(grad_z, "xh")
    grad_z = halving_scatter(grad_z, "y")
    grad_y = lax.psum_scatter(grad_y, "z", scatter_dimension=0, tiled=True)
    grad_y = halving_scatter(grad_y, "xh")
    grad = jnp.concatenate([grad_z, grad_y], axis=1)
    grad = grad * scale
    drift = island_drift[0]
    first = beta_one * moment1[0] + (1.0 - beta_one) * grad
    second = beta_two * moment2[0] + (1.0 - beta_two) * grad * grad
    step = first / (jnp.sqrt(second) + epsilon) + decay_rate * (global_params - drift)
    pseudo = drift + inner_rate * step
    pair_core = [(i, i ^ 1) for i in range(island_count)]
    pair_chip = [(i, i ^ 2) for i in range(island_count)]
    summed = pseudo + lax.ppermute(pseudo, "island", pair_core)
    summed = summed + lax.ppermute(summed, "island", pair_chip)
    mean = summed / island_count
    new_momentum = nesterov * momentum + mean
    new_global = global_params - outer_rate * (mean + nesterov * new_momentum)
    weights = new_global.astype(jnp.bfloat16)
    core = lax.axis_index("island") % 2
    half = weights.shape[1] // 2
    own = lax.dynamic_slice_in_dim(weights, core * half, half, axis=1)
    own_full = doubling_gather(own, "y")
    own_full = doubling_gather(own_full, "xh")
    own_full = lax.all_gather(own_full, "z", axis=0, tiled=True)
    other_full = lax.ppermute(own_full, "island", pair_core)
    keys_own = jnp.dot(acts_perm, own_full, preferred_element_type=jnp.float32)
    keys_other = jnp.dot(acts_perm, other_full, preferred_element_type=jnp.float32)
    keys_own = (keys_own * D ** (-0.5)).astype(jnp.bfloat16)
    keys_other = (keys_other * D ** (-0.5)).astype(jnp.bfloat16)
    is_first = core == 0
    keys = jnp.concatenate(
        [jnp.where(is_first, keys_own, keys_other), jnp.where(is_first, keys_other, keys_own)],
        axis=1,
    )
    return (keys, new_global, new_momentum, first[None], second[None])


def solution(mesh):
    fsdp_n = mesh.shape["fsdp"]
    mesh = Mesh(mesh.devices.reshape(mesh.shape["island"], 2, 8, fsdp_n // 16), ("island",) + FS)
    return jax.shard_map(
        per_device,
        mesh=mesh,
        in_specs=(
            P(("island", *FS), None),
            P(("island", *FS), None),
            P(FS, None),
            P(FS, None),
            P("island", FS, None),
            P("island", FS, None),
            P("island", FS, None),
        ),
        out_specs=(
            P(("island", *FS), None),
            P(FS, None),
            P(FS, None),
            P("island", FS, None),
            P("island", FS, None),
        ),
        check_vma=False,
    )
```

```python
import jax
import jax.numpy as jnp
from jax import lax
from jax.sharding import Mesh, PartitionSpec as P

D = 8192
FS = ("xh", "z", "y")


beta_one = 0.9
beta_two = 0.95
epsilon = 1e-08
inner_rate = 0.05
decay_rate = 0.1
outer_rate = 0.7
nesterov = 0.9


def ring_scatter(x, axis):
    n = lax.axis_size(axis)
    me = lax.axis_index(axis)
    chunk = x.shape[0] // n
    h = x.shape[1] // 2
    parts = []
    for sign, cols in ((1, slice(0, h)), (-1, slice(h, None))):
        data = x[:, cols]
        perm = [(i, (i + sign) % n) for i in range(n)]
        pick = lambda k: lax.dynamic_slice_in_dim(data, (k % n) * chunk, chunk, axis=0)
        acc = pick(me - sign + n)
        for s in range(n - 1):
            acc = lax.ppermute(acc, axis, perm) + pick(me - sign * (2 + s) + 2 * n)
        parts.append(acc)
    return jnp.concatenate(parts, axis=1)


def halving_scatter(x, axis):
    n = lax.axis_size(axis)
    me = lax.axis_index(axis)
    bit = n // 2
    while bit >= 1:
        half = x.shape[0] // 2
        mine = (me // bit) % 2
        keep = lax.dynamic_slice_in_dim(x, mine * half, half, axis=0)
        send = lax.dynamic_slice_in_dim(x, (1 - mine) * half, half, axis=0)
        recv = lax.ppermute(send, axis, [(i, i ^ bit) for i in range(n)])
        x = keep + recv
        bit //= 2
    return x


def doubling_gather(x, axis):
    n = lax.axis_size(axis)
    me = lax.axis_index(axis)
    bit = 1
    while bit < n:
        recv = lax.ppermute(x, axis, [(i, i ^ bit) for i in range(n)])
        low = (me // bit) % 2 == 0
        x = jnp.where(low, jnp.concatenate([x, recv], 0), jnp.concatenate([recv, x], 0))
        bit *= 2
    return x


def per_device(acts, cotangent, global_params, momentum, island_drift, moment1, moment2):
    fsdp_count = lax.axis_size(FS)
    island_count = lax.axis_size("island")
    scale = (acts.shape[0] * fsdp_count) ** (-0.5)
    xh_n, z_n, y_n = (lax.axis_size(a) for a in ("xh", "z", "y"))
    tokens = acts.shape[0]
    blocks = acts.reshape(tokens, xh_n, z_n, y_n, D // (xh_n * z_n * y_n))
    acts_perm = blocks.transpose(0, 2, 1, 3, 4).reshape(tokens, D)
    acts_yfirst = blocks.transpose(0, 3, 2, 1, 4).reshape(tokens, D)
    cols = cotangent.shape[1] // 2
    dims = (((0,), (0,)), ((), ()))
    part_z = lax.dot_general(acts_perm, cotangent[:, :cols], dims, preferred_element_type=jnp.float32)
    part_y = lax.dot_general(acts_yfirst, cotangent[:, cols:], dims, preferred_element_type=jnp.float32)
    grad_z = lax.psum_scatter(part_z, "z", scatter_dimension=0, tiled=True)
    grad_y = ring_scatter(part_y, "y")
    grad_z = halving_scatter(grad_z, "xh")
    grad_z = halving_scatter(grad_z, "y")
    grad_y = lax.psum_scatter(grad_y, "z", scatter_dimension=0, tiled=True)
    grad_y = halving_scatter(grad_y, "xh")
    grad = jnp.concatenate([grad_z, grad_y], axis=1)
    grad = grad * scale
    drift = island_drift[0]
    first = beta_one * moment1[0] + (1.0 - beta_one) * grad
    second = beta_two * moment2[0] + (1.0 - beta_two) * grad * grad
    step = first / (jnp.sqrt(second) + epsilon) + decay_rate * (global_params - drift)
    pseudo = drift + inner_rate * step
    pair_core = [(i, i ^ 1) for i in range(island_count)]
    pair_chip = [(i, i ^ 2) for i in range(island_count)]
    summed = pseudo + lax.ppermute(pseudo, "island", pair_core)
    summed = summed + lax.ppermute(summed, "island", pair_chip)
    mean = summed / island_count
    new_momentum = nesterov * momentum + mean
    new_global = global_params - outer_rate * (mean + nesterov * new_momentum)
    weights = new_global.astype(jnp.bfloat16)
    core = lax.axis_index("island") % 2
    half = weights.shape[1] // 2
    own = lax.dynamic_slice_in_dim(weights, core * half, half, axis=1)
    quarter = half // 2
    full_p = doubling_gather(own[:, :quarter], "y")
    full_p = doubling_gather(full_p, "xh")
    full_p = lax.all_gather(full_p, "z", axis=0, tiled=True)
    acts_q = blocks.transpose(0, 1, 3, 2, 4).reshape(tokens, D)
    full_q = lax.all_gather(own[:, quarter:], "z", axis=0, tiled=True)
    full_q = doubling_gather(full_q, "y")
    full_q = doubling_gather(full_q, "xh")
    other_p = lax.ppermute(full_p, "island", pair_core)
    other_q = lax.ppermute(full_q, "island", pair_core)
    dot = lambda a, w: jnp.dot(a, w, preferred_element_type=jnp.float32)
    keys_own = jnp.concatenate([dot(acts_perm, full_p), dot(acts_q, full_q)], axis=1)
    keys_other = jnp.concatenate([dot(acts_perm, other_p), dot(acts_q, other_q)], axis=1)
    keys_own = (keys_own * D ** (-0.5)).astype(jnp.bfloat16)
    keys_other = (keys_other * D ** (-0.5)).astype(jnp.bfloat16)
    is_first = core == 0
    keys = jnp.concatenate(
        [jnp.where(is_first, keys_own, keys_other), jnp.where(is_first, keys_other, keys_own)],
        axis=1,
    )
    return (keys, new_global, new_momentum, first[None], second[None])


def solution(mesh):
    fsdp_n = mesh.shape["fsdp"]
    mesh = Mesh(mesh.devices.reshape(mesh.shape["island"], 2, 8, fsdp_n // 16), ("island",) + FS)
    return jax.shard_map(
        per_device,
        mesh=mesh,
        in_specs=(
            P(("island", *FS), None),
            P(("island", *FS), None),
            P(FS, None),
            P(FS, None),
            P("island", FS, None),
            P("island", FS, None),
            P("island", FS, None),
        ),
        out_specs=(
            P(("island", *FS), None),
            P(FS, None),
            P(FS, None),
            P("island", FS, None),
            P("island", FS, None),
        ),
        check_vma=False,
    )
```

```python
import jax
import jax.numpy as jnp
from jax import lax
from jax.sharding import Mesh, PartitionSpec as P

D = 8192
FS = ("xh", "z", "y")


beta_one = 0.9
beta_two = 0.95
epsilon = 1e-08
inner_rate = 0.05
decay_rate = 0.1
outer_rate = 0.7
nesterov = 0.9


def ring_scatter(x, axis):
    n = lax.axis_size(axis)
    me = lax.axis_index(axis)
    chunk = x.shape[0] // n
    h = x.shape[1] // 2
    parts = []
    for sign, cols in ((1, slice(0, h)), (-1, slice(h, None))):
        data = x[:, cols]
        perm = [(i, (i + sign) % n) for i in range(n)]
        pick = lambda k: lax.dynamic_slice_in_dim(data, (k % n) * chunk, chunk, axis=0)
        acc = pick(me - sign + n)
        for s in range(n - 1):
            acc = lax.ppermute(acc, axis, perm) + pick(me - sign * (2 + s) + 2 * n)
        parts.append(acc)
    return jnp.concatenate(parts, axis=1)


def halving_scatter(x, axis):
    n = lax.axis_size(axis)
    me = lax.axis_index(axis)
    bit = n // 2
    while bit >= 1:
        half = x.shape[0] // 2
        mine = (me // bit) % 2
        keep = lax.dynamic_slice_in_dim(x, mine * half, half, axis=0)
        send = lax.dynamic_slice_in_dim(x, (1 - mine) * half, half, axis=0)
        recv = lax.ppermute(send, axis, [(i, i ^ bit) for i in range(n)])
        x = keep + recv
        bit //= 2
    return x


def doubling_gather(x, axis):
    n = lax.axis_size(axis)
    me = lax.axis_index(axis)
    bit = 1
    while bit < n:
        recv = lax.ppermute(x, axis, [(i, i ^ bit) for i in range(n)])
        low = (me // bit) % 2 == 0
        x = jnp.where(low, jnp.concatenate([x, recv], 0), jnp.concatenate([recv, x], 0))
        bit *= 2
    return x


def per_device(acts, cotangent, global_params, momentum, island_drift, moment1, moment2):
    fsdp_count = lax.axis_size(FS)
    island_count = lax.axis_size("island")
    scale = (acts.shape[0] * fsdp_count) ** (-0.5)
    xh_n, z_n, y_n = (lax.axis_size(a) for a in ("xh", "z", "y"))
    tokens = acts.shape[0]
    blocks = acts.reshape(tokens, xh_n, z_n, y_n, D // (xh_n * z_n * y_n))
    acts_perm = blocks.transpose(0, 2, 1, 3, 4).reshape(tokens, D)
    acts_yfirst = blocks.transpose(0, 3, 2, 1, 4).reshape(tokens, D)
    cols = cotangent.shape[1] // 2
    dims = (((0,), (0,)), ((), ()))
    part_z = lax.dot_general(acts_perm, cotangent[:, :cols], dims, preferred_element_type=jnp.float32)
    part_y = lax.dot_general(acts_yfirst, cotangent[:, cols:], dims, preferred_element_type=jnp.float32)
    grad_z = lax.psum_scatter(part_z, "z", scatter_dimension=0, tiled=True)
    grad_y = ring_scatter(part_y, "y")
    grad_z = halving_scatter(grad_z, "xh")
    grad_z = halving_scatter(grad_z, "y")
    grad_y = lax.psum_scatter(grad_y, "z", scatter_dimension=0, tiled=True)
    grad_y = halving_scatter(grad_y, "xh")
    drift_all = island_drift[0]
    pair_core = [(i, i ^ 1) for i in range(island_count)]
    pair_chip = [(i, i ^ 2) for i in range(island_count)]
    firsts, seconds, sums = [], [], []
    for g, cs in ((grad_z, slice(0, cols)), (grad_y, slice(cols, None))):
        g = g * scale
        drift = drift_all[:, cs]
        first = beta_one * moment1[0][:, cs] + (1.0 - beta_one) * g
        second = beta_two * moment2[0][:, cs] + (1.0 - beta_two) * g * g
        step = first / (jnp.sqrt(second) + epsilon) + decay_rate * (global_params[:, cs] - drift)
        pseudo = drift + inner_rate * step
        summed = pseudo + lax.ppermute(pseudo, "island", pair_core)
        summed = summed + lax.ppermute(summed, "island", pair_chip)
        firsts.append(first)
        seconds.append(second)
        sums.append(summed)
    first = jnp.concatenate(firsts, axis=1)
    second = jnp.concatenate(seconds, axis=1)
    summed = jnp.concatenate(sums, axis=1)
    mean = summed / island_count
    new_momentum = nesterov * momentum + mean
    new_global = global_params - outer_rate * (mean + nesterov * new_momentum)
    weights = new_global.astype(jnp.bfloat16)
    core = lax.axis_index("island") % 2
    half = weights.shape[1] // 2
    own = lax.dynamic_slice_in_dim(weights, core * half, half, axis=1)
    own_full = doubling_gather(own, "y")
    own_full = doubling_gather(own_full, "xh")
    own_full = lax.all_gather(own_full, "z", axis=0, tiled=True)
    other_full = lax.ppermute(own_full, "island", pair_core)
    keys_own = jnp.dot(acts_perm, own_full, preferred_element_type=jnp.float32)
    keys_other = jnp.dot(acts_perm, other_full, preferred_element_type=jnp.float32)
    keys_own = (keys_own * D ** (-0.5)).astype(jnp.bfloat16)
    keys_other = (keys_other * D ** (-0.5)).astype(jnp.bfloat16)
    is_first = core == 0
    keys = jnp.concatenate(
        [jnp.where(is_first, keys_own, keys_other), jnp.where(is_first, keys_other, keys_own)],
        axis=1,
    )
    return (keys, new_global, new_momentum, first[None], second[None])


def solution(mesh):
    fsdp_n = mesh.shape["fsdp"]
    mesh = Mesh(mesh.devices.reshape(mesh.shape["island"], 2, 8, fsdp_n // 16), ("island",) + FS)
    return jax.shard_map(
        per_device,
        mesh=mesh,
        in_specs=(
            P(("island", *FS), None),
            P(("island", *FS), None),
            P(FS, None),
            P(FS, None),
            P("island", FS, None),
            P("island", FS, None),
            P("island", FS, None),
        ),
        out_specs=(
            P(("island", *FS), None),
            P(FS, None),
            P(FS, None),
            P("island", FS, None),
            P("island", FS, None),
        ),
        check_vma=False,
    )
```
